256 devices in a mesh: shard: 8 (over z), tensor: 4 (over y), section: 8 (over x, core).
Axes of the slice: x: 4, y: 4, z: 8, core: 2. Of those that a mesh axis runs over, the one named last changes fastest.
Arguments:
- emb_grad: float32 [960, 32000], P(('tensor', 'section'), 'shard'), may hold values from -60 to 60
- mlp_grad: float32 [3, 960, 2560], P(None, ('tensor', 'section'), 'shard'), may hold values from -60 to 60
- emb_basis: float32 [960, 256], P(('tensor', 'section')), may hold values from -0.1875 to 0.1875
- mlp_basis: float32 [3, 960, 256], P(None, ('tensor', 'section')), may hold values from -0.1875 to 0.1875
- emb_first: float32 [256, 32000], P(('tensor', 'section'), 'shard'), may hold values from -6 to 6
- emb_second: float32 [256, 32000], P(('tensor', 'section'), 'shard'), may hold values from 0.002 to 0.05
- mlp_first: float32 [256, 3, 2560], P(('tensor', 'section'), None, 'shard'), may hold values from -6 to 6
- mlp_second: float32 [256, 3, 2560], P(('tensor', 'section'), None, 'shard'), may hold values from 0.002 to 0.05
Outputs:
- emb_update: float32 [960, 32000], P(('tensor', 'section'), 'shard')
- mlp_update: float32 [3, 960, 2560], P(None, ('tensor', 'section'), 'shard')
- emb_first_new: float32 [256, 32000], P(('tensor', 'section'), 'shard')
- emb_second_new: float32 [256, 32000], P(('tensor', 'section'), 'shard')
- mlp_first_new: float32 [256, 3, 2560], P(('tensor', 'section'), None, 'shard')
- mlp_second_new: float32 [256, 3, 2560], P(('tensor', 'section'), None, 'shard')
- emb_basis_new: float32 [960, 256], P(('tensor', 'section'))
- mlp_basis_new: float32 [3, 960, 256], P(None, ('tensor', 'section'))
The draws below stay inside these ranges and needn't reach their ends.
All inputs are finite; a program needn't handle non-finite values.
Results may differ from the reference program's by a relative error of at most 0.0003.
Values sent between devices are 32-bit elements; how exact they have to be, the bound alone decides.
No kernel may reach another device: no remote copies, remote signals or barrier semaphores. Data moves between devices by JAX's collectives and lax.ppermute only.
A program may use at most 64 MiB of HBM per device.

```python
import math
import jax
import jax.numpy as jnp
from jax import lax

D = 960
FF = 2560
V = 32000
RANK = 256
MATS = 3
NS_STEPS = 3


def spread_field(key, leading, row_count, column_count):
    noise_key, row_key, column_key = jax.random.split(key, 3)
    full_shape = (leading, row_count, column_count)
    noise = jnp.clip(jax.random.normal(noise_key, full_shape, jnp.float32), -6.0, 6.0)
    top_level = math.log(10.0)
    row_scale = jnp.exp(jax.random.uniform(row_key, (leading, row_count, 1), jnp.float32, 0.0, top_level))
    column_scale = jnp.exp(jax.random.uniform(column_key, (leading, 1, column_count), jnp.float32, 0.0, top_level))
    return noise * row_scale * column_scale / 20.0


def draw_emb_grad(key, part):
    return spread_field(key, 1, D, V)[0]


def draw_mlp_grad(key, part):
    return spread_field(key, MATS, D, FF)


def levels(own_key, extent, shards, smallest, high):
    def one(axis_at, blocks):
        heights = jax.random.uniform(jax.random.fold_in(jax.random.fold_in(own_key, 6), axis_at), (blocks,), jnp.float32, smallest / len(shards), high / len(shards))
        return jnp.repeat(jnp.exp(heights), extent[axis_at] // blocks).reshape((-1,) + (1,) * (len(extent) - axis_at - 1))

    level = one(*shards[0])
    for cut in shards[1:]:
        level = level * one(*cut)
    return level


def bell_draw(rng, extent, width, bound, cuts=(), kind=jnp.bfloat16):
    factor_of = levels(rng, extent, cuts, -0.22, 0.18) if cuts else 1.0
    array = jax.random.normal(rng, extent, jnp.float32) * width * factor_of
    return jnp.minimum(jnp.maximum(array, -bound), bound).astype(kind)


def setup_inputs(seed: int = 0) -> dict:
    splits = jax.random.split(jax.random.key(seed), 9)
    return {
        "emb_grad": draw_emb_grad(jax.random.fold_in(splits[8], 71), 0),
        "mlp_grad": draw_mlp_grad(jax.random.fold_in(splits[8], 71), 0),
        "emb_basis": bell_draw(splits[2], (D, RANK), D ** -0.5, 0.1875, ((0, 32),), jnp.float32),
        "mlp_basis": bell_draw(splits[3], (MATS, D, RANK), D ** -0.5, 0.1875, ((1, 32),), jnp.float32),
        "emb_first": bell_draw(splits[4], (RANK, V), 1.0, 6.0, ((0, 32), (1, 8)), jnp.float32),
        "emb_second": jnp.clip(jnp.exp(math.log(0.05) - 3.218876 * jax.random.uniform(splits[5], (RANK, V), jnp.float32) ** levels(splits[5], (RANK, V), ((0, 32), (1, 8)), -0.2, 0.2)), 0.002, 0.05),
        "mlp_first": bell_draw(splits[6], (RANK, MATS, FF), 1.0, 6.0, ((0, 32), (2, 8)), jnp.float32),
        "mlp_second": jnp.clip(jnp.exp(math.log(0.05) - 3.218876 * jax.random.uniform(splits[7], (RANK, MATS, FF), jnp.float32) ** levels(splits[7], (RANK, MATS, FF), ((0, 32), (2, 8)), -0.2, 0.2)), 0.002, 0.05),
    }


coef_a = 3.4445
coef_b = -4.775
coef_c = 2.0315
bias_one = 1.0 - 0.9 ** 10
bias_two = 1.0 - 0.999 ** 10
adam_eps = 1e-08
norm_eps = 1e-07
highest = lax.Precision.HIGHEST

def adam_moments(first, second, projected):
    first_new = 0.9 * first + 0.1 * projected
    second_new = 0.999 * second + 0.001 * projected * projected
    direction = first_new / bias_one / (jnp.sqrt(second_new / bias_two) + adam_eps)
    return (first_new, second_new, direction)

def orthogonalize(target):
    norm_value = jnp.sqrt(jnp.sum(target * target)) + norm_eps
    current = target / norm_value
    for sweep_index in range(NS_STEPS):
        gram_term = jnp.dot(current.T, current, precision=highest)
        polynomial = coef_b * gram_term + coef_c * jnp.dot(gram_term, gram_term, precision=highest)
        current = coef_a * current + jnp.dot(current, polynomial, precision=highest)
    return current

def reference(emb_grad, mlp_grad, emb_basis, mlp_basis, emb_first, emb_second, mlp_first, mlp_second):
    emb_small = jnp.dot(emb_basis.T, emb_grad, precision=highest)
    mlp_small = jnp.einsum('kdr,kdf->rkf', mlp_basis, mlp_grad, precision=highest)
    emb_first_new, emb_second_new, emb_direction = adam_moments(emb_first, emb_second, emb_small)
    mlp_first_new, mlp_second_new, mlp_direction = adam_moments(mlp_first, mlp_second, mlp_small)
    emb_update = jnp.dot(emb_basis, emb_direction, precision=highest)
    mlp_update = jnp.einsum('kdr,rkf->kdf', mlp_basis, mlp_direction, precision=highest)
    emb_target = jnp.dot(emb_grad, emb_small.T, precision=highest)
    mlp_target = jnp.einsum('kdf,rkf->kdr', mlp_grad, mlp_small, precision=highest)
    emb_basis_new = orthogonalize(emb_target)
    mlp_basis_new = jax.vmap(orthogonalize)(mlp_target)
    return (emb_update, mlp_update, emb_first_new, emb_second_new, mlp_first_new, mlp_second_new, emb_basis_new, mlp_basis_new)
```

```python
import jax
import jax.numpy as jnp
from jax import lax
from jax.sharding import PartitionSpec as P

NS_STEPS = 3


coef_a = 3.4445
coef_b = -4.775
coef_c = 2.0315
bias_one = 1.0 - 0.9**10
bias_two = 1.0 - 0.999**10
adam_eps = 1e-08
norm_eps = 1e-07
highest = lax.Precision.HIGHEST


def adam_moments(first, second, projected):
    first_new = 0.9 * first + 0.1 * projected
    second_new = 0.999 * second + 0.001 * projected * projected
    direction = first_new / bias_one / (jnp.sqrt(second_new / bias_two) + adam_eps)
    return (first_new, second_new, direction)


def newton_schulz(target, gram):
    squares = jnp.trace(gram, axis1=-2, axis2=-1)
    scale = 1.0 / (jnp.sqrt(squares) + norm_eps)
    gram_term = gram * (scale * scale)[..., None, None]
    eye = jnp.eye(gram.shape[-1], dtype=gram.dtype)
    total = None
    for sweep_index in range(NS_STEPS):
        factor = coef_a * eye + polish_poly(gram_term)
        if sweep_index + 1 < NS_STEPS:
            gram_term = jnp.einsum(
                "...rs,...st->...rt",
                factor,
                jnp.einsum("...rs,...st->...rt", gram_term, factor, precision=highest),
                precision=highest,
            )
        total = factor if total is None else jnp.einsum(
            "...rs,...st->...rt", total, factor, precision=highest
        )
    current = target * scale[..., None, None]
    return jnp.einsum("...dr,...rs->...ds", current, total, precision=highest)


def polish_poly(gram_term):
    return coef_b * gram_term + coef_c * jnp.einsum(
        "...rs,...st->...rt", gram_term, gram_term, precision=highest
    )


def gram_sums(emb_iterate, mlp_iterate):
    emb_gram = jnp.einsum("dr,ds->rs", emb_iterate, emb_iterate, precision=highest)
    mlp_gram = jnp.einsum("kdr,kds->krs", mlp_iterate, mlp_iterate, precision=highest)
    return lax.psum((emb_gram, mlp_gram), ("tensor", "section"))


def local_terms(emb_grad, mlp_grad, emb_basis, mlp_basis):
    emb_term = jnp.einsum("dr,dv->rv", emb_basis, emb_grad, precision=highest)
    mlp_term = jnp.einsum("kdr,kdf->rkf", mlp_basis, mlp_grad, precision=highest)
    return (emb_term, mlp_term)


def project_back(emb_basis, mlp_basis, emb_total, mlp_total, emb_piece, mlp_piece):
    emb_total = jnp.dot(emb_basis, emb_piece, precision=highest)
    mlp_total = jnp.einsum("kdr,rkf->kdf", mlp_basis, mlp_piece, precision=highest)
    return (emb_total, mlp_total)


def local(emb_grad, mlp_grad, emb_basis, mlp_basis, emb_first, emb_second, mlp_first, mlp_second):
    emb_term, mlp_term = local_terms(emb_grad, mlp_grad, emb_basis, mlp_basis)
    emb_zero = jnp.zeros(emb_grad.shape, jnp.float32)
    mlp_zero = jnp.zeros(mlp_grad.shape, jnp.float32)
    emb_share, mlp_share = (
        lax.psum_scatter(emb_term, ("tensor", "section"), scatter_dimension=0, tiled=True),
        lax.psum_scatter(mlp_term, ("tensor", "section"), scatter_dimension=0, tiled=True),
    )
    emb_first_new, emb_second_new, emb_direction = adam_moments(emb_first, emb_second, emb_share)
    mlp_first_new, mlp_second_new, mlp_direction = adam_moments(mlp_first, mlp_second, mlp_share)
    emb_total = emb_zero
    mlp_total = mlp_zero
    emb_piece = lax.all_gather(emb_direction, ("tensor", "section"), axis=0, tiled=True)
    emb_projected = lax.all_gather(emb_share, ("tensor", "section"), axis=0, tiled=True)
    mlp_piece = lax.all_gather(mlp_direction, ("tensor", "section"), axis=0, tiled=True)
    mlp_projected = lax.all_gather(mlp_share, ("tensor", "section"), axis=0, tiled=True)
    emb_total, mlp_total = project_back(
        emb_basis, mlp_basis, emb_total, mlp_total, emb_piece, mlp_piece
    )
    emb_found_block = jnp.einsum("dv,rv->dr", emb_grad, emb_projected, precision=highest)
    mlp_found_block = jnp.einsum("kdf,rkf->kdr", mlp_grad, mlp_projected, precision=highest)
    emb_part, mlp_part = lax.psum((emb_found_block, mlp_found_block), "shard")
    emb_gram, mlp_gram = gram_sums(emb_part, mlp_part)
    emb_iterate = newton_schulz(emb_part, emb_gram)
    mlp_iterate = newton_schulz(mlp_part, mlp_gram)
    return (
        emb_total,
        mlp_total,
        emb_first_new,
        emb_second_new,
        mlp_first_new,
        mlp_second_new,
        emb_iterate,
        mlp_iterate,
    )


def solution(mesh):
    placed = (
        P(("tensor", "section"), "shard"),
        P(None, ("tensor", "section"), "shard"),
        P(("tensor", "section"), None),
        P(None, ("tensor", "section"), None),
        P(("tensor", "section"), "shard"),
        P(("tensor", "section"), "shard"),
        P(("tensor", "section"), None, "shard"),
        P(("tensor", "section"), None, "shard"),
    )
    return jax.shard_map(
        local,
        mesh=mesh,
        in_specs=placed,
        out_specs=(
            P(("tensor", "section"), "shard"),
            P(None, ("tensor", "section"), "shard"),
            P(("tensor", "section"), "shard"),
            P(("tensor", "section"), "shard"),
            P(("tensor", "section"), None, "shard"),
            P(("tensor", "section"), None, "shard"),
            P(("tensor", "section"), None),
            P(None, ("tensor", "section"), None),
        ),
        check_vma=False,
    )
```

```python
import jax
import jax.numpy as jnp
from jax import lax
from jax.sharding import PartitionSpec as P

NS_STEPS = 3


coef_a = 3.4445
coef_b = -4.775
coef_c = 2.0315
bias_one = 1.0 - 0.9**10
bias_two = 1.0 - 0.999**10
adam_eps = 1e-08
norm_eps = 1e-07
highest = lax.Precision.HIGHEST
WIDE = ("tensor", "section")


def adam_moments(first, second, projected):
    first_new = 0.9 * first + 0.1 * projected
    second_new = 0.999 * second + 0.001 * projected * projected
    direction = first_new / bias_one / (jnp.sqrt(second_new / bias_two) + adam_eps)
    return (first_new, second_new, direction)


def matmul(x, y):
    return jnp.einsum("...rs,...st->...rt", x, y, precision=highest)


def newton_schulz(target, gram):
    squares = jnp.trace(gram, axis1=-2, axis2=-1)
    scale = 1.0 / (jnp.sqrt(squares) + norm_eps)
    gram_term = gram * (scale * scale)[..., None, None]
    eye = jnp.broadcast_to(jnp.eye(gram.shape[-1], dtype=gram.dtype), gram.shape)

    def sweep(_, carry):
        gram_term, total = carry
        factor = coef_a * eye + coef_b * gram_term + coef_c * matmul(gram_term, gram_term)
        return (matmul(factor, matmul(gram_term, factor)), matmul(total, factor))

    _, total = lax.fori_loop(0, NS_STEPS, sweep, (gram_term, eye))
    current = target * scale[..., None, None]
    return matmul(current, total)


def local(emb_grad, mlp_grad, emb_basis, mlp_basis, emb_first, emb_second, mlp_first, mlp_second):
    mats, rows, cols = mlp_grad.shape
    long_side = emb_grad.shape[1]
    rank = emb_basis.shape[1]
    emb_term = jnp.einsum("dr,dv->rv", emb_basis, emb_grad, precision=highest)
    mlp_term = jnp.einsum("kdr,kdf->rkf", mlp_basis, mlp_grad, precision=highest)
    terms = jnp.concatenate([emb_term, mlp_term.reshape(rank, mats * cols)], axis=1)
    pad = -terms.shape[1] % 512
    terms = jnp.pad(terms, ((0, 0), (0, pad)))
    share = lax.psum_scatter(terms, WIDE, scatter_dimension=0, tiled=True)
    emb_share = share[:, :long_side]
    mlp_share = share[:, long_side : long_side + mats * cols].reshape(-1, mats, cols)
    emb_first_new, emb_second_new, emb_direction = adam_moments(emb_first, emb_second, emb_share)
    mlp_first_new, mlp_second_new, mlp_direction = adam_moments(mlp_first, mlp_second, mlp_share)
    pieces = jnp.concatenate(
        [
            emb_direction,
            mlp_direction.reshape(-1, mats * cols),
            share[:, : long_side + mats * cols],
        ],
        axis=1,
    )
    gathered = lax.all_gather(pieces, WIDE, axis=0, tiled=True)
    width = long_side + mats * cols
    emb_piece = gathered[:, :long_side]
    mlp_piece = gathered[:, long_side:width].reshape(rank, mats, cols)
    emb_projected = gathered[:, width : width + long_side]
    mlp_projected = gathered[:, width + long_side :].reshape(rank, mats, cols)
    emb_total = jnp.dot(emb_basis, emb_piece, precision=highest)
    mlp_total = jnp.einsum("kdr,rkf->kdf", mlp_basis, mlp_piece, precision=highest)
    emb_found = jnp.einsum("dv,rv->dr", emb_grad, emb_projected, precision=highest)
    mlp_found = jnp.einsum("kdf,rkf->dkr", mlp_grad, mlp_projected, precision=highest)
    found = jnp.concatenate([emb_found, mlp_found.reshape(rows, mats * rank)], axis=1)
    found = lax.psum(found, "shard")
    every = lax.all_gather(found, WIDE, axis=0, tiled=True)
    every = every.reshape(-1, mats + 1, rank).transpose(1, 0, 2)
    gram = jnp.einsum("kdr,kds->krs", every, every, precision=highest)
    targets = found.reshape(rows, mats + 1, rank).transpose(1, 0, 2)
    basis_new = newton_schulz(targets, gram)
    return (
        emb_total,
        mlp_total,
        emb_first_new,
        emb_second_new,
        mlp_first_new,
        mlp_second_new,
        basis_new[0],
        basis_new[1:],
    )


def solution(mesh):
    placed = (
        P(WIDE, "shard"),
        P(None, WIDE, "shard"),
        P(WIDE, None),
        P(None, WIDE, None),
        P(WIDE, "shard"),
        P(WIDE, "shard"),
        P(WIDE, None, "shard"),
        P(WIDE, None, "shard"),
    )
    return jax.shard_map(
        local,
        mesh=mesh,
        in_specs=placed,
        out_specs=(
            P(WIDE, "shard"),
            P(None, WIDE, "shard"),
            P(WIDE, "shard"),
            P(WIDE, "shard"),
            P(WIDE, None, "shard"),
            P(WIDE, None, "shard"),
            P(WIDE, None),
            P(None, WIDE, None),
        ),
        check_vma=False,
    )
```

```python
import functools

import jax
import jax.numpy as jnp
from jax import lax
from jax.sharding import PartitionSpec as P

NS_STEPS = 3


coef_a = 3.4445
coef_b = -4.775
coef_c = 2.0315
bias_one = 1.0 - 0.9**10
bias_two = 1.0 - 0.999**10
adam_eps = 1e-08
norm_eps = 1e-07
highest = lax.Precision.HIGHEST
WIDE = ("tensor", "section")


def adam_moments(first, second, projected):
    first_new = 0.9 * first + 0.1 * projected
    second_new = 0.999 * second + 0.001 * projected * projected
    direction = first_new / bias_one / (jnp.sqrt(second_new / bias_two) + adam_eps)
    return (first_new, second_new, direction)


def matmul(x, y):
    return jnp.einsum("...rs,...st->...rt", x, y, precision=highest)


def newton_schulz(target, gram):
    squares = jnp.trace(gram, axis1=-2, axis2=-1)
    scale = 1.0 / (jnp.sqrt(squares) + norm_eps)
    gram_term = gram * (scale * scale)[..., None, None]
    eye = jnp.broadcast_to(jnp.eye(gram.shape[-1], dtype=gram.dtype), gram.shape)

    def sweep(_, carry):
        gram_term, total = carry
        factor = coef_a * eye + coef_b * gram_term + coef_c * matmul(gram_term, gram_term)
        return (matmul(factor, matmul(gram_term, factor)), matmul(total, factor))

    _, total = lax.fori_loop(0, NS_STEPS, sweep, (gram_term, eye))
    current = target * scale[..., None, None]
    return matmul(current, total)


def exchange_sum(value, axis, count):
    if count & (count - 1):
        return lax.psum(value, axis)
    step = 1
    while step < count:
        pairs = [(index, index ^ step) for index in range(count)]
        value = value + lax.ppermute(value, axis, pairs)
        step *= 2
    return value


def local(shard_count, emb_grad, mlp_grad, emb_basis, mlp_basis, emb_first, emb_second, mlp_first, mlp_second):
    mats, rows, cols = mlp_grad.shape
    long_side = emb_grad.shape[1]
    rank = emb_basis.shape[1]
    emb_term = jnp.einsum("dr,dv->rv", emb_basis, emb_grad, precision=highest)
    mlp_term = jnp.einsum("kdr,kdf->rkf", mlp_basis, mlp_grad, precision=highest)
    terms = jnp.concatenate([emb_term, mlp_term.reshape(rank, mats * cols)], axis=1)
    pad = -terms.shape[1] % 512
    terms = jnp.pad(terms, ((0, 0), (0, pad)))
    share = lax.psum_scatter(terms, WIDE, scatter_dimension=0, tiled=True)
    emb_share = share[:, :long_side]
    mlp_share = share[:, long_side : long_side + mats * cols].reshape(-1, mats, cols)
    emb_first_new, emb_second_new, emb_direction = adam_moments(emb_first, emb_second, emb_share)
    mlp_first_new, mlp_second_new, mlp_direction = adam_moments(mlp_first, mlp_second, mlp_share)
    pieces = jnp.concatenate(
        [
            emb_direction,
            mlp_direction.reshape(-1, mats * cols),
            share[:, : long_side + mats * cols],
        ],
        axis=1,
    )
    gathered = lax.all_gather(pieces, WIDE, axis=0, tiled=True)
    width = long_side + mats * cols
    emb_piece = gathered[:, :long_side]
    mlp_piece = gathered[:, long_side:width].reshape(rank, mats, cols)
    emb_projected = gathered[:, width : width + long_side]
    mlp_projected = gathered[:, width + long_side :].reshape(rank, mats, cols)
    emb_total = jnp.dot(emb_basis, emb_piece, precision=highest)
    mlp_total = jnp.einsum("kdr,rkf->kdf", mlp_basis, mlp_piece, precision=highest)
    emb_found = jnp.einsum("dv,rv->dr", emb_grad, emb_projected, precision=highest)
    mlp_found = jnp.einsum("kdf,rkf->dkr", mlp_grad, mlp_projected, precision=highest)
    found = jnp.concatenate([emb_found, mlp_found.reshape(rows, mats * rank)], axis=1)
    found = exchange_sum(found, "shard", shard_count)
    every = lax.all_gather(found, WIDE, axis=0, tiled=True)
    every = every.reshape(-1, mats + 1, rank).transpose(1, 0, 2)
    gram = jnp.einsum("kdr,kds->krs", every, every, precision=highest)
    targets = found.reshape(rows, mats + 1, rank).transpose(1, 0, 2)
    basis_new = newton_schulz(targets, gram)
    return (
        emb_total,
        mlp_total,
        emb_first_new,
        emb_second_new,
        mlp_first_new,
        mlp_second_new,
        basis_new[0],
        basis_new[1:],
    )


def solution(mesh):
    placed = (
        P(WIDE, "shard"),
        P(None, WIDE, "shard"),
        P(WIDE, None),
        P(None, WIDE, None),
        P(WIDE, "shard"),
        P(WIDE, "shard"),
        P(WIDE, None, "shard"),
        P(WIDE, None, "shard"),
    )
    return jax.shard_map(
        functools.partial(local, mesh.shape["shard"]),
        mesh=mesh,
        in_specs=placed,
        out_specs=(
            P(WIDE, "shard"),
            P(None, WIDE, "shard"),
            P(WIDE, "shard"),
            P(WIDE, "shard"),
            P(WIDE, None, "shard"),
            P(WIDE, None, "shard"),
            P(WIDE, None),
            P(None, WIDE, None),
        ),
        check_vma=False,
    )
```

```python
import functools

import jax
import jax.numpy as jnp
from jax import lax
from jax.sharding import PartitionSpec as P

NS_STEPS = 3


coef_a = 3.4445
coef_b = -4.775
coef_c = 2.0315
bias_one = 1.0 - 0.9**10
bias_two = 1.0 - 0.999**10
adam_eps = 1e-08
norm_eps = 1e-07
highest = lax.Precision.HIGHEST
WIDE = ("tensor", "section")


def adam_moments(first, second, projected):
    first_new = 0.9 * first + 0.1 * projected
    second_new = 0.999 * second + 0.001 * projected * projected
    direction = first_new / bias_one / (jnp.sqrt(second_new / bias_two) + adam_eps)
    return (first_new, second_new, direction)


def matmul(x, y):
    return jnp.einsum("...rs,...st->...rt", x, y, precision=highest)


def newton_schulz(target, gram):
    squares = jnp.trace(gram, axis1=-2, axis2=-1)
    scale = 1.0 / (jnp.sqrt(squares) + norm_eps)
    gram_term = gram * (scale * scale)[..., None, None]
    eye = jnp.broadcast_to(jnp.eye(gram.shape[-1], dtype=gram.dtype), gram.shape)

    def sweep(_, carry):
        gram_term, total = carry
        factor = coef_a * eye + coef_b * gram_term + coef_c * matmul(gram_term, gram_term)
        return (matmul(factor, matmul(gram_term, factor)), matmul(total, factor))

    _, total = lax.fori_loop(0, NS_STEPS, sweep, (gram_term, eye))
    current = target * scale[..., None, None]
    return matmul(current, total)


def exchange_sum(value, axis, count):
    if count & (count - 1):
        return lax.psum(value, axis)
    step = 1
    while step < count:
        pairs = [(index, index ^ step) for index in range(count)]
        value = value + lax.ppermute(value, axis, pairs)
        step *= 2
    return value


def halving_scatter(value, axis, count):
    if count & (count - 1):
        return lax.psum_scatter(value, axis, scatter_dimension=0, tiled=True)
    bits = count.bit_length() - 1
    block = value.shape[0] // count
    index = lax.axis_index(axis)
    value = value.reshape((2,) * bits + (block,) + value.shape[1:])
    for bit in range(bits):
        own = (index >> bit) & 1
        axis_at = bits - 1 - bit
        keep = lax.dynamic_index_in_dim(value, own, axis_at, keepdims=False)
        send = lax.dynamic_index_in_dim(value, 1 - own, axis_at, keepdims=False)
        pairs = [(place, place ^ (1 << bit)) for place in range(count)]
        value = keep + lax.ppermute(send, axis, pairs)
    return value


def local(shard_count, wide_count, emb_grad, mlp_grad, emb_basis, mlp_basis, emb_first, emb_second, mlp_first, mlp_second):
    mats, rows, cols = mlp_grad.shape
    long_side = emb_grad.shape[1]
    rank = emb_basis.shape[1]
    emb_term = jnp.einsum("dr,dv->rv", emb_basis, emb_grad, precision=highest)
    mlp_term = jnp.einsum("kdr,kdf->rkf", mlp_basis, mlp_grad, precision=highest)
    terms = jnp.concatenate([emb_term, mlp_term.reshape(rank, mats * cols)], axis=1)
    share = halving_scatter(terms, WIDE, wide_count)
    emb_share = share[:, :long_side]
    mlp_share = share[:, long_side : long_side + mats * cols].reshape(-1, mats, cols)
    emb_first_new, emb_second_new, emb_direction = adam_moments(emb_first, emb_second, emb_share)
    mlp_first_new, mlp_second_new, mlp_direction = adam_moments(mlp_first, mlp_second, mlp_share)
    pieces = jnp.concatenate(
        [
            emb_direction,
            mlp_direction.reshape(-1, mats * cols),
            share,
        ],
        axis=1,
    )
    gathered = lax.all_gather(pieces, WIDE, axis=0, tiled=True)
    width = long_side + mats * cols
    emb_piece = gathered[:, :long_side]
    mlp_piece = gathered[:, long_side:width].reshape(rank, mats, cols)
    emb_projected = gathered[:, width : width + long_side]
    mlp_projected = gathered[:, width + long_side :].reshape(rank, mats, cols)
    emb_total = jnp.dot(emb_basis, emb_piece, precision=highest)
    mlp_total = jnp.einsum("kdr,rkf->kdf", mlp_basis, mlp_piece, precision=highest)
    emb_found = jnp.einsum("dv,rv->dr", emb_grad, emb_projected, precision=highest)
    mlp_found = jnp.einsum("kdf,rkf->dkr", mlp_grad, mlp_projected, precision=highest)
    found = jnp.concatenate([emb_found, mlp_found.reshape(rows, mats * rank)], axis=1)
    found = exchange_sum(found, "shard", shard_count)
    every = lax.all_gather(found, WIDE, axis=0, tiled=True)
    every = every.reshape(-1, mats + 1, rank).transpose(1, 0, 2)
    gram = jnp.einsum("kdr,kds->krs", every, every, precision=highest)
    targets = found.reshape(rows, mats + 1, rank).transpose(1, 0, 2)
    basis_new = newton_schulz(targets, gram)
    return (
        emb_total,
        mlp_total,
        emb_first_new,
        emb_second_new,
        mlp_first_new,
        mlp_second_new,
        basis_new[0],
        basis_new[1:],
    )


def solution(mesh):
    placed = (
        P(WIDE, "shard"),
        P(None, WIDE, "shard"),
        P(WIDE, None),
        P(None, WIDE, None),
        P(WIDE, "shard"),
        P(WIDE, "shard"),
        P(WIDE, None, "shard"),
        P(WIDE, None, "shard"),
    )
    return jax.shard_map(
        functools.partial(local, mesh.shape["shard"], mesh.shape["tensor"] * mesh.shape["section"]),
        mesh=mesh,
        in_specs=placed,
        out_specs=(
            P(WIDE, "shard"),
            P(None, WIDE, "shard"),
            P(WIDE, "shard"),
            P(WIDE, "shard"),
            P(WIDE, None, "shard"),
            P(WIDE, None, "shard"),
            P(WIDE, None),
            P(None, WIDE, None),
        ),
        check_vma=False,
    )
```

```python
import functools

import jax
import jax.numpy as jnp
from jax import lax
from jax.sharding import PartitionSpec as P

NS_STEPS = 3


coef_a = 3.4445
coef_b = -4.775
coef_c = 2.0315
bias_one = 1.0 - 0.9**10
bias_two = 1.0 - 0.999**10
adam_eps = 1e-08
norm_eps = 1e-07
matmul_precision = lax.Precision.HIGH
WIDE = ("tensor", "section")


def adam_moments(first, second, projected):
    first_new = 0.9 * first + 0.1 * projected
    second_new = 0.999 * second + 0.001 * projected * projected
    direction = first_new / bias_one / (jnp.sqrt(second_new / bias_two) + adam_eps)
    return (first_new, second_new, direction)


def matmul(x, y):
    return jnp.einsum("...rs,...st->...rt", x, y, precision=matmul_precision)


def newton_schulz(target, gram):
    squares = jnp.trace(gram, axis1=-2, axis2=-1)
    scale = 1.0 / (jnp.sqrt(squares) + norm_eps)
    gram_term = gram * (scale * scale)[..., None, None]
    eye = jnp.broadcast_to(jnp.eye(gram.shape[-1], dtype=gram.dtype), gram.shape)

    def sweep(_, carry):
        gram_term, total = carry
        factor = coef_a * eye + coef_b * gram_term + coef_c * matmul(gram_term, gram_term)
        return (matmul(factor, matmul(gram_term, factor)), matmul(total, factor))

    _, total = lax.fori_loop(0, NS_STEPS, sweep, (gram_term, eye))
    current = target * scale[..., None, None]
    return matmul(current, total)


def exchange_sum(value, axis, count):
    if count & (count - 1):
        return lax.psum(value, axis)
    step = 1
    while step < count:
        pairs = [(index, index ^ step) for index in range(count)]
        value = value + lax.ppermute(value, axis, pairs)
        step *= 2
    return value


def halving_scatter(value, axis, count):
    if count & (count - 1):
        return lax.psum_scatter(value, axis, scatter_dimension=0, tiled=True)
    bits = count.bit_length() - 1
    block = value.shape[0] // count
    index = lax.axis_index(axis)
    value = value.reshape((2,) * bits + (block,) + value.shape[1:])
    for bit in range(bits):
        own = (index >> bit) & 1
        axis_at = bits - 1 - bit
        keep = lax.dynamic_index_in_dim(value, own, axis_at, keepdims=False)
        send = lax.dynamic_index_in_dim(value, 1 - own, axis_at, keepdims=False)
        pairs = [(place, place ^ (1 << bit)) for place in range(count)]
        value = keep + lax.ppermute(send, axis, pairs)
    return value


def local(shard_count, wide_count, emb_grad, mlp_grad, emb_basis, mlp_basis, emb_first, emb_second, mlp_first, mlp_second):
    mats, rows, cols = mlp_grad.shape
    long_side = emb_grad.shape[1]
    rank = emb_basis.shape[1]
    emb_term = jnp.einsum("dr,dv->rv", emb_basis, emb_grad, precision=matmul_precision)
    mlp_term = jnp.einsum("kdr,kdf->rkf", mlp_basis, mlp_grad, precision=matmul_precision)
    terms = jnp.concatenate([emb_term, mlp_term.reshape(rank, mats * cols)], axis=1)
    share = halving_scatter(terms, WIDE, wide_count)
    emb_share = share[:, :long_side]
    mlp_share = share[:, long_side : long_side + mats * cols].reshape(-1, mats, cols)
    emb_first_new, emb_second_new, emb_direction = adam_moments(emb_first, emb_second, emb_share)
    mlp_first_new, mlp_second_new, mlp_direction = adam_moments(mlp_first, mlp_second, mlp_share)
    pieces = jnp.concatenate(
        [
            emb_direction,
            mlp_direction.reshape(-1, mats * cols),
            share,
        ],
        axis=1,
    )
    gathered = lax.all_gather(pieces, WIDE, axis=0, tiled=True)
    width = long_side + mats * cols
    emb_piece = gathered[:, :long_side]
    mlp_piece = gathered[:, long_side:width].reshape(rank, mats, cols)
    emb_projected = gathered[:, width : width + long_side]
    mlp_projected = gathered[:, width + long_side :].reshape(rank, mats, cols)
    emb_total = jnp.dot(emb_basis, emb_piece, precision=matmul_precision)
    mlp_total = jnp.einsum("kdr,rkf->kdf", mlp_basis, mlp_piece, precision=matmul_precision)
    emb_found = jnp.einsum("dv,rv->dr", emb_grad, emb_projected, precision=matmul_precision)
    mlp_found = jnp.einsum("kdf,rkf->dkr", mlp_grad, mlp_projected, precision=matmul_precision)
    found = jnp.concatenate([emb_found, mlp_found.reshape(rows, mats * rank)], axis=1)
    found = exchange_sum(found, "shard", shard_count)
    every = lax.all_gather(found, WIDE, axis=0, tiled=True)
    every = every.reshape(-1, mats + 1, rank).transpose(1, 0, 2)
    gram = jnp.einsum("kdr,kds->krs", every, every, precision=matmul_precision)
    targets = found.reshape(rows, mats + 1, rank).transpose(1, 0, 2)
    basis_new = newton_schulz(targets, gram)
    return (
        emb_total,
        mlp_total,
        emb_first_new,
        emb_second_new,
        mlp_first_new,
        mlp_second_new,
        basis_new[0],
        basis_new[1:],
    )


def solution(mesh):
    placed = (
        P(WIDE, "shard"),
        P(None, WIDE, "shard"),
        P(WIDE, None),
        P(None, WIDE, None),
        P(WIDE, "shard"),
        P(WIDE, "shard"),
        P(WIDE, None, "shard"),
        P(WIDE, None, "shard"),
    )
    return jax.shard_map(
        functools.partial(local, mesh.shape["shard"], mesh.shape["tensor"] * mesh.shape["section"]),
        mesh=mesh,
        in_specs=placed,
        out_specs=(
            P(WIDE, "shard"),
            P(None, WIDE, "shard"),
            P(WIDE, "shard"),
            P(WIDE, "shard"),
            P(WIDE, None, "shard"),
            P(WIDE, None, "shard"),
            P(WIDE, None),
            P(None, WIDE, None),
        ),
        check_vma=False,
    )
```

```python
import functools

import jax
import jax.numpy as jnp
from jax import lax
from jax.sharding import PartitionSpec as P

NS_STEPS = 3


coef_a = 3.4445
coef_b = -4.775
coef_c = 2.0315
bias_one = 1.0 - 0.9**10
bias_two = 1.0 - 0.999**10
adam_eps = 1e-08
norm_eps = 1e-07
matmul_precision = lax.Precision.HIGH
WIDE = ("tensor", "section")


def adam_moments(first, second, projected):
    first_new = 0.9 * first + 0.1 * projected
    second_new = 0.999 * second + 0.001 * projected * projected
    direction = first_new / bias_one / (jnp.sqrt(second_new / bias_two) + adam_eps)
    return (first_new, second_new, direction)


def matmul(x, y):
    return jnp.einsum("...rs,...st->...rt", x, y, precision=matmul_precision)


def newton_schulz(target, gram):
    squares = jnp.trace(gram, axis1=-2, axis2=-1)
    scale = 1.0 / (jnp.sqrt(squares) + norm_eps)
    gram_term = gram * (scale * scale)[..., None, None]
    eye = jnp.broadcast_to(jnp.eye(gram.shape[-1], dtype=gram.dtype), gram.shape)

    def sweep(_, carry):
        gram_term, total = carry
        factor = coef_a * eye + coef_b * gram_term + coef_c * matmul(gram_term, gram_term)
        return (matmul(factor, matmul(gram_term, factor)), matmul(total, factor))

    _, total = lax.fori_loop(0, NS_STEPS, sweep, (gram_term, eye))
    current = target * scale[..., None, None]
    return matmul(current, total)


def exchange_sum(value, axis, count):
    if count & (count - 1):
        return lax.psum(value, axis)
    step = 1
    while step < count:
        pairs = [(index, index ^ step) for index in range(count)]
        value = value + lax.ppermute(value, axis, pairs)
        step *= 2
    return value


def halving_scatter(value, axis, count, split_at):
    if count & (count - 1):
        return lax.psum_scatter(value, axis, scatter_dimension=0, tiled=True)
    bits = count.bit_length() - 1
    block = value.shape[0] // count
    index = lax.axis_index(axis)
    value = value.reshape((2,) * bits + (block,) + value.shape[1:])
    value, remaining = halving_step(value, list(range(bits - 1, -1, -1)), 0, axis, count, index)
    if bits < 2:
        return value
    cut = value.shape[-1] // 2
    low = list(range(1, split_at))
    high = list(range(split_at, bits))
    first, first_left = value[..., :cut], remaining
    second, second_left = value[..., cut:], remaining
    for bit_a, bit_b in zip(low + high, high + low):
        first, first_left = halving_step(first, first_left, bit_a, axis, count, index)
        second, second_left = halving_step(second, second_left, bit_b, axis, count, index)
    return jnp.concatenate([first, second], axis=-1)


def halving_step(value, remaining, bit, axis, count, index):
    own = (index >> bit) & 1
    axis_at = remaining.index(bit)
    keep = lax.dynamic_index_in_dim(value, own, axis_at, keepdims=False)
    send = lax.dynamic_index_in_dim(value, 1 - own, axis_at, keepdims=False)
    pairs = [(place, place ^ (1 << bit)) for place in range(count)]
    left = [other for other in remaining if other != bit]
    return keep + lax.ppermute(send, axis, pairs), left


def local(shard_count, wide_count, split_at, emb_grad, mlp_grad, emb_basis, mlp_basis, emb_first, emb_second, mlp_first, mlp_second):
    mats, rows, cols = mlp_grad.shape
    long_side = emb_grad.shape[1]
    rank = emb_basis.shape[1]
    emb_term = jnp.einsum("dr,dv->rv", emb_basis, emb_grad, precision=matmul_precision)
    mlp_term = jnp.einsum("kdr,kdf->rkf", mlp_basis, mlp_grad, precision=matmul_precision)
    terms = jnp.concatenate([emb_term, mlp_term.reshape(rank, mats * cols)], axis=1)
    share = halving_scatter(terms, WIDE, wide_count, split_at)
    emb_share = share[:, :long_side]
    mlp_share = share[:, long_side : long_side + mats * cols].reshape(-1, mats, cols)
    emb_first_new, emb_second_new, emb_direction = adam_moments(emb_first, emb_second, emb_share)
    mlp_first_new, mlp_second_new, mlp_direction = adam_moments(mlp_first, mlp_second, mlp_share)
    pieces = jnp.concatenate(
        [
            emb_direction,
            mlp_direction.reshape(-1, mats * cols),
            share,
        ],
        axis=1,
    )
    gathered = lax.all_gather(pieces, WIDE, axis=0, tiled=True)
    width = long_side + mats * cols
    emb_piece = gathered[:, :long_side]
    mlp_piece = gathered[:, long_side:width].reshape(rank, mats, cols)
    emb_projected = gathered[:, width : width + long_side]
    mlp_projected = gathered[:, width + long_side :].reshape(rank, mats, cols)
    emb_total = jnp.dot(emb_basis, emb_piece, precision=matmul_precision)
    mlp_total = jnp.einsum("kdr,rkf->kdf", mlp_basis, mlp_piece, precision=matmul_precision)
    emb_found = jnp.einsum("dv,rv->dr", emb_grad, emb_projected, precision=matmul_precision)
    mlp_found = jnp.einsum("kdf,rkf->dkr", mlp_grad, mlp_projected, precision=matmul_precision)
    found = jnp.concatenate([emb_found, mlp_found.reshape(rows, mats * rank)], axis=1)
    found = exchange_sum(found, "shard", shard_count)
    every = lax.all_gather(found, WIDE, axis=0, tiled=True)
    every = every.reshape(-1, mats + 1, rank).transpose(1, 0, 2)
    gram = jnp.einsum("kdr,kds->krs", every, every, precision=matmul_precision)
    targets = found.reshape(rows, mats + 1, rank).transpose(1, 0, 2)
    basis_new = newton_schulz(targets, gram)
    return (
        emb_total,
        mlp_total,
        emb_first_new,
        emb_second_new,
        mlp_first_new,
        mlp_second_new,
        basis_new[0],
        basis_new[1:],
    )


def solution(mesh):
    placed = (
        P(WIDE, "shard"),
        P(None, WIDE, "shard"),
        P(WIDE, None),
        P(None, WIDE, None),
        P(WIDE, "shard"),
        P(WIDE, "shard"),
        P(WIDE, None, "shard"),
        P(WIDE, None, "shard"),
    )
    return jax.shard_map(
        functools.partial(
            local,
            mesh.shape["shard"],
            mesh.shape["tensor"] * mesh.shape["section"],
            (mesh.shape["section"]).bit_length() - 1,
        ),
        mesh=mesh,
        in_specs=placed,
        out_specs=(
            P(WIDE, "shard"),
            P(None, WIDE, "shard"),
            P(WIDE, "shard"),
            P(WIDE, "shard"),
            P(WIDE, None, "shard"),
            P(WIDE, None, "shard"),
            P(WIDE, None),
            P(None, WIDE, None),
        ),
        check_vma=False,
    )
```

```python
import functools

import jax
import jax.numpy as jnp
from jax import lax
from jax.sharding import PartitionSpec as P

NS_STEPS = 3


coef_a = 3.4445
coef_b = -4.775
coef_c = 2.0315
bias_one = 1.0 - 0.9**10
bias_two = 1.0 - 0.999**10
adam_eps = 1e-08
norm_eps = 1e-07
matmul_precision = lax.Precision.HIGH
WIDE = ("tensor", "section")


def adam_moments(first, second, projected):
    first_new = 0.9 * first + 0.1 * projected
    second_new = 0.999 * second + 0.001 * projected * projected
    direction = first_new / bias_one / (jnp.sqrt(second_new / bias_two) + adam_eps)
    return (first_new, second_new, direction)


def matmul(x, y):
    return jnp.einsum("...rs,...st->...rt", x, y, precision=matmul_precision)


def newton_schulz(target, gram):
    squares = jnp.trace(gram, axis1=-2, axis2=-1)
    scale = 1.0 / (jnp.sqrt(squares) + norm_eps)
    gram_term = gram * (scale * scale)[..., None, None]
    eye = jnp.broadcast_to(jnp.eye(gram.shape[-1], dtype=gram.dtype), gram.shape)

    def sweep(_, carry):
        gram_term, total = carry
        factor = coef_a * eye + coef_b * gram_term + coef_c * matmul(gram_term, gram_term)
        return (matmul(factor, matmul(gram_term, factor)), matmul(total, factor))

    _, total = lax.fori_loop(0, NS_STEPS, sweep, (gram_term, eye))
    current = target * scale[..., None, None]
    return matmul(current, total)


def exchange_sum(value, axis, count):
    if count & (count - 1):
        return lax.psum(value, axis)
    step = 1
    while step < count:
        pairs = [(index, index ^ step) for index in range(count)]
        value = value + lax.ppermute(value, axis, pairs)
        step *= 2
    return value


def halving_scatter(value, axis, count, split_at):
    if count & (count - 1):
        return lax.psum_scatter(value, axis, scatter_dimension=0, tiled=True)
    bits = count.bit_length() - 1
    block = value.shape[0] // count
    index = lax.axis_index(axis)
    value = value.reshape((2,) * bits + (block,) + value.shape[1:])
    value, remaining = halving_step(value, list(range(bits - 1, -1, -1)), 0, axis, count, index)
    if bits < 2:
        return value
    cut = value.shape[-1] // 2
    low = list(range(1, split_at))
    high = list(range(split_at, bits))
    first, first_left = value[..., :cut], remaining
    second, second_left = value[..., cut:], remaining
    for bit_a, bit_b in zip(low + high, high + low):
        first, first_left = halving_step(first, first_left, bit_a, axis, count, index)
        second, second_left = halving_step(second, second_left, bit_b, axis, count, index)
    return jnp.concatenate([first, second], axis=-1)


def halving_step(value, remaining, bit, axis, count, index):
    own = (index >> bit) & 1
    axis_at = remaining.index(bit)
    keep = lax.dynamic_index_in_dim(value, own, axis_at, keepdims=False)
    send = lax.dynamic_index_in_dim(value, 1 - own, axis_at, keepdims=False)
    pairs = [(place, place ^ (1 << bit)) for place in range(count)]
    left = [other for other in remaining if other != bit]
    return keep + lax.ppermute(send, axis, pairs), left


def swap(value, axis):
    return lax.all_to_all(value, axis, 0, 0, tiled=True)


def local(shard_count, wide_count, split_at, emb_grad, mlp_grad, emb_basis, mlp_basis, emb_first, emb_second, mlp_first, mlp_second):
    mats, rows, cols = mlp_grad.shape
    long_side = emb_grad.shape[1]
    rank = emb_basis.shape[1]
    part = rank // wide_count
    emb_cut = long_side // wide_count
    mlp_cut = cols // wide_count
    group = emb_cut + mats * mlp_cut

    def to_groups(emb_value, mlp_value):
        lead = emb_value.shape[0]
        emb_value = emb_value.reshape(lead, wide_count, emb_cut)
        mlp_value = mlp_value.reshape(mats, lead, wide_count, mlp_cut).transpose(1, 2, 0, 3)
        mlp_value = mlp_value.reshape(lead, wide_count, mats * mlp_cut)
        return jnp.concatenate([emb_value, mlp_value], axis=2).transpose(1, 0, 2)

    def from_groups(value):
        lead = value.shape[1]
        value = value.transpose(1, 0, 2)
        emb_value = value[:, :, :emb_cut].reshape(lead, long_side)
        mlp_value = value[:, :, emb_cut:].reshape(lead, wide_count, mats, mlp_cut)
        mlp_value = mlp_value.transpose(2, 0, 1, 3).reshape(mats, lead, cols)
        return emb_value, mlp_value

    bases = jnp.concatenate([emb_basis[:, None], mlp_basis.transpose(1, 0, 2)], axis=1)
    bases = lax.all_gather(bases, WIDE, axis=0, tiled=True)
    grads = swap(to_groups(emb_grad, mlp_grad), WIDE).reshape(rows * wide_count, group)
    mlp_first_by_mat = mlp_first.transpose(1, 0, 2)
    mlp_second_by_mat = mlp_second.transpose(1, 0, 2)
    moments = jnp.concatenate(
        [to_groups(emb_first, mlp_first_by_mat), to_groups(emb_second, mlp_second_by_mat)], axis=2
    )
    moments = swap(moments, WIDE).reshape(rank, 2 * group)
    first = moments[:, :group]
    second = moments[:, group:]

    emb_cols = grads[:, :emb_cut]
    mlp_cols = grads[:, emb_cut:].reshape(-1, mats, mlp_cut)
    emb_small = jnp.einsum("dr,dc->rc", bases[:, 0], emb_cols, precision=matmul_precision)
    mlp_small = jnp.einsum("dkr,dkc->rkc", bases[:, 1:], mlp_cols, precision=matmul_precision)
    small = jnp.concatenate([emb_small, mlp_small.reshape(rank, mats * mlp_cut)], axis=1)
    first_new, second_new, direction = adam_moments(first, second, small)
    emb_update = jnp.einsum(
        "dr,rc->dc", bases[:, 0], direction[:, :emb_cut], precision=matmul_precision
    )
    mlp_update = jnp.einsum(
        "dkr,rkc->dkc",
        bases[:, 1:],
        direction[:, emb_cut:].reshape(rank, mats, mlp_cut),
        precision=matmul_precision,
    )
    updates = jnp.concatenate([emb_update, mlp_update.reshape(-1, mats * mlp_cut)], axis=1)
    back_moments = swap(
        jnp.concatenate([first_new, second_new], axis=1).reshape(wide_count, part, 2 * group), WIDE
    )
    emb_first_new, mlp_first_new = from_groups(back_moments[:, :, :group])
    emb_second_new, mlp_second_new = from_groups(back_moments[:, :, group:])
    back_updates = swap(updates.reshape(wide_count, rows, group), WIDE)
    emb_total, mlp_total = from_groups(back_updates)

    emb_found = jnp.einsum("dc,rc->dr", emb_cols, emb_small, precision=matmul_precision)
    mlp_found = jnp.einsum("dkc,rkc->dkr", mlp_cols, mlp_small, precision=matmul_precision)
    found = jnp.concatenate([emb_found[:, None], mlp_found], axis=1).reshape(-1, (mats + 1) * rank)
    found = halving_scatter(found, WIDE, wide_count, split_at)
    found = exchange_sum(found, "shard", shard_count)
    every = lax.all_gather(found, WIDE, axis=0, tiled=True)
    every = every.reshape(-1, mats + 1, rank).transpose(1, 0, 2)
    gram = jnp.einsum("kdr,kds->krs", every, every, precision=matmul_precision)
    targets = found.reshape(rows, mats + 1, rank).transpose(1, 0, 2)
    basis_new = newton_schulz(targets, gram)
    return (
        emb_total,
        mlp_total,
        emb_first_new,
        emb_second_new,
        mlp_first_new.transpose(1, 0, 2),
        mlp_second_new.transpose(1, 0, 2),
        basis_new[0],
        basis_new[1:],
    )


def solution(mesh):
    placed = (
        P(WIDE, "shard"),
        P(None, WIDE, "shard"),
        P(WIDE, None),
        P(None, WIDE, None),
        P(WIDE, "shard"),
        P(WIDE, "shard"),
        P(WIDE, None, "shard"),
        P(WIDE, None, "shard"),
    )
    return jax.shard_map(
        functools.partial(
            local,
            mesh.shape["shard"],
            mesh.shape["tensor"] * mesh.shape["section"],
            (mesh.shape["section"]).bit_length() - 1,
        ),
        mesh=mesh,
        in_specs=placed,
        out_specs=(
            P(WIDE, "shard"),
            P(None, WIDE, "shard"),
            P(WIDE, "shard"),
            P(WIDE, "shard"),
            P(WIDE, None, "shard"),
            P(WIDE, None, "shard"),
            P(WIDE, None),
            P(None, WIDE, None),
        ),
        check_vma=False,
    )
```

```python
import functools

import jax
import jax.numpy as jnp
from jax import lax
from jax.sharding import PartitionSpec as P

NS_STEPS = 3


coef_a = 3.4445
coef_b = -4.775
coef_c = 2.0315
bias_one = 1.0 - 0.9**10
bias_two = 1.0 - 0.999**10
adam_eps = 1e-08
norm_eps = 1e-07
matmul_precision = lax.Precision.HIGH
WIDE = ("tensor", "section")


def adam_moments(first, second, projected):
    first_new = 0.9 * first + 0.1 * projected
    second_new = 0.999 * second + 0.001 * projected * projected
    direction = first_new / bias_one / (jnp.sqrt(second_new / bias_two) + adam_eps)
    return (first_new, second_new, direction)


def matmul(x, y):
    return jnp.einsum("...rs,...st->...rt", x, y, precision=matmul_precision)


def newton_schulz(target, gram):
    squares = jnp.trace(gram, axis1=-2, axis2=-1)
    scale = 1.0 / (jnp.sqrt(squares) + norm_eps)
    gram_term = gram * (scale * scale)[..., None, None]
    eye = jnp.broadcast_to(jnp.eye(gram.shape[-1], dtype=gram.dtype), gram.shape)

    def sweep(_, carry):
        gram_term, total = carry
        factor = coef_a * eye + coef_b * gram_term + coef_c * matmul(gram_term, gram_term)
        return (matmul(factor, matmul(gram_term, factor)), matmul(total, factor))

    _, total = lax.fori_loop(0, NS_STEPS, sweep, (gram_term, eye))
    current = target * scale[..., None, None]
    return matmul(current, total)


def exchange_sum(value, axis, count):
    if count & (count - 1):
        return lax.psum(value, axis)
    step = 1
    while step < count:
        pairs = [(index, index ^ step) for index in range(count)]
        value = value + lax.ppermute(value, axis, pairs)
        step *= 2
    return value


def halving_scatter(value, axis, count, split_at):
    if count & (count - 1):
        return lax.psum_scatter(value, axis, scatter_dimension=0, tiled=True)
    bits = count.bit_length() - 1
    block = value.shape[0] // count
    index = lax.axis_index(axis)
    value = value.reshape((2,) * bits + (block,) + value.shape[1:])
    value, remaining = halving_step(value, list(range(bits - 1, -1, -1)), 0, axis, count, index)
    if bits < 2:
        return value
    cut = value.shape[-1] // 2
    low = list(range(1, split_at))
    high = list(range(split_at, bits))
    first, first_left = value[..., :cut], remaining
    second, second_left = value[..., cut:], remaining
    for bit_a, bit_b in zip(low + high, high + low):
        first, first_left = halving_step(first, first_left, bit_a, axis, count, index)
        second, second_left = halving_step(second, second_left, bit_b, axis, count, index)
    return jnp.concatenate([first, second], axis=-1)


def halving_step(value, remaining, bit, axis, count, index):
    own = (index >> bit) & 1
    axis_at = remaining.index(bit)
    keep = lax.dynamic_index_in_dim(value, own, axis_at, keepdims=False)
    send = lax.dynamic_index_in_dim(value, 1 - own, axis_at, keepdims=False)
    pairs = [(place, place ^ (1 << bit)) for place in range(count)]
    left = [other for other in remaining if other != bit]
    return keep + lax.ppermute(send, axis, pairs), left


def local(shard_count, wide_count, split_at, emb_grad, mlp_grad, emb_basis, mlp_basis, emb_first, emb_second, mlp_first, mlp_second):
    mats, rows, cols = mlp_grad.shape
    long_side = emb_grad.shape[1]
    rank = emb_basis.shape[1]
    emb_term = jnp.einsum("dr,dv->rv", emb_basis, emb_grad, precision=matmul_precision)
    mlp_term = jnp.einsum("kdr,kdf->rkf", mlp_basis, mlp_grad, precision=matmul_precision)
    terms = jnp.concatenate([emb_term, mlp_term.reshape(rank, mats * cols)], axis=1)
    share = halving_scatter(terms, WIDE, wide_count, split_at)
    emb_share = share[:, :long_side]
    mlp_share = share[:, long_side : long_side + mats * cols].reshape(-1, mats, cols)
    emb_first_new, emb_second_new, emb_direction = adam_moments(emb_first, emb_second, emb_share)
    mlp_first_new, mlp_second_new, mlp_direction = adam_moments(mlp_first, mlp_second, mlp_share)
    pieces = jnp.concatenate(
        [
            emb_direction,
            mlp_direction.reshape(-1, mats * cols),
            share,
        ],
        axis=1,
    )
    gathered = lax.all_gather(pieces, WIDE, axis=0, tiled=True)
    width = long_side + mats * cols
    emb_piece = gathered[:, :long_side]
    mlp_piece = gathered[:, long_side:width].reshape(rank, mats, cols)
    emb_projected = gathered[:, width : width + long_side]
    mlp_projected = gathered[:, width + long_side :].reshape(rank, mats, cols)
    emb_total = jnp.dot(emb_basis, emb_piece, precision=matmul_precision)
    mlp_total = jnp.einsum("kdr,rkf->kdf", mlp_basis, mlp_piece, precision=matmul_precision)
    emb_found = jnp.einsum("dv,rv->dr", emb_grad, emb_projected, precision=matmul_precision)
    mlp_found = jnp.einsum("kdf,rkf->dkr", mlp_grad, mlp_projected, precision=matmul_precision)
    found = jnp.concatenate([emb_found, mlp_found.reshape(rows, mats * rank)], axis=1)
    found = exchange_sum(found, "shard", shard_count)
    every = lax.all_gather(found, WIDE, axis=0)
    every = jnp.einsum("tdr,tds->rs", every, every, precision=matmul_precision)
    gram = jnp.stack(
        [every[k * rank : (k + 1) * rank, k * rank : (k + 1) * rank] for k in range(mats + 1)]
    )
    targets = found.reshape(rows, mats + 1, rank).transpose(1, 0, 2)
    basis_new = newton_schulz(targets, gram)
    return (
        emb_total,
        mlp_total,
        emb_first_new,
        emb_second_new,
        mlp_first_new,
        mlp_second_new,
        basis_new[0],
        basis_new[1:],
    )


def solution(mesh):
    placed = (
        P(WIDE, "shard"),
        P(None, WIDE, "shard"),
        P(WIDE, None),
        P(None, WIDE, None),
        P(WIDE, "shard"),
        P(WIDE, "shard"),
        P(WIDE, None, "shard"),
        P(WIDE, None, "shard"),
    )
    return jax.shard_map(
        functools.partial(
            local,
            mesh.shape["shard"],
            mesh.shape["tensor"] * mesh.shape["section"],
            (mesh.shape["section"]).bit_length() - 1,
        ),
        mesh=mesh,
        in_specs=placed,
        out_specs=(
            P(WIDE, "shard"),
            P(None, WIDE, "shard"),
            P(WIDE, "shard"),
            P(WIDE, "shard"),
            P(WIDE, None, "shard"),
            P(WIDE, None, "shard"),
            P(WIDE, None),
            P(None, WIDE, None),
        ),
        check_vma=False,
    )
```

```python
import functools

import jax
import jax.numpy as jnp
from jax import lax
from jax.sharding import PartitionSpec as P

NS_STEPS = 3


coef_a = 3.4445
coef_b = -4.775
coef_c = 2.0315
bias_one = 1.0 - 0.9**10
bias_two = 1.0 - 0.999**10
adam_eps = 1e-08
norm_eps = 1e-07
matmul_precision = lax.Precision.HIGH
WIDE = ("tensor", "section")


def adam_moments(first, second, projected):
    first_new = 0.9 * first + 0.1 * projected
    second_new = 0.999 * second + 0.001 * projected * projected
    direction = first_new / bias_one / (jnp.sqrt(second_new / bias_two) + adam_eps)
    return (first_new, second_new, direction)


def matmul(x, y):
    return jnp.einsum("...rs,...st->...rt", x, y, precision=matmul_precision)


def newton_schulz(target, gram):
    squares = jnp.trace(gram, axis1=-2, axis2=-1)
    scale = 1.0 / (jnp.sqrt(squares) + norm_eps)
    gram_term = gram * (scale * scale)[..., None, None]
    eye = jnp.broadcast_to(jnp.eye(gram.shape[-1], dtype=gram.dtype), gram.shape)

    def sweep(_, carry):
        gram_term, total = carry
        factor = coef_a * eye + coef_b * gram_term + coef_c * matmul(gram_term, gram_term)
        return (matmul(factor, matmul(gram_term, factor)), matmul(total, factor))

    _, total = lax.fori_loop(0, NS_STEPS, sweep, (gram_term, eye))
    current = target * scale[..., None, None]
    return matmul(current, total)


def exchange_sum(value, axis, count):
    if count & (count - 1):
        return lax.psum(value, axis)
    step = 1
    while step < count:
        pairs = [(index, index ^ step) for index in range(count)]
        value = value + lax.ppermute(value, axis, pairs)
        step *= 2
    return value


def halving_scatter(value, axis, count, split_at):
    if count & (count - 1):
        return lax.psum_scatter(value, axis, scatter_dimension=0, tiled=True)
    bits = count.bit_length() - 1
    block = value.shape[0] // count
    index = lax.axis_index(axis)
    value = value.reshape((2,) * bits + (block,) + value.shape[1:])
    value, remaining = halving_step(value, list(range(bits - 1, -1, -1)), 0, axis, count, index)
    if bits < 2:
        return value
    cut = value.shape[-1] // 2
    low = list(range(1, split_at))
    high = list(range(split_at, bits))
    first, first_left = value[..., :cut], remaining
    second, second_left = value[..., cut:], remaining
    for bit_a, bit_b in zip(low + high, high + low):
        first, first_left = halving_step(first, first_left, bit_a, axis, count, index)
        second, second_left = halving_step(second, second_left, bit_b, axis, count, index)
    return jnp.concatenate([first, second], axis=-1)


def halving_step(value, remaining, bit, axis, count, index):
    own = (index >> bit) & 1
    axis_at = remaining.index(bit)
    keep = lax.dynamic_index_in_dim(value, own, axis_at, keepdims=False)
    send = lax.dynamic_index_in_dim(value, 1 - own, axis_at, keepdims=False)
    pairs = [(place, place ^ (1 << bit)) for place in range(count)]
    left = [other for other in remaining if other != bit]
    return keep + lax.ppermute(send, axis, pairs), left


def local(shard_count, wide_count, split_at, emb_grad, mlp_grad, emb_basis, mlp_basis, emb_first, emb_second, mlp_first, mlp_second):
    mats, rows, cols = mlp_grad.shape
    long_side = emb_grad.shape[1]
    rank = emb_basis.shape[1]
    emb_term = jnp.einsum("dr,dv->rv", emb_basis, emb_grad, precision=matmul_precision)
    mlp_term = jnp.einsum("kdr,kdf->rkf", mlp_basis, mlp_grad, precision=matmul_precision)
    terms = jnp.concatenate([emb_term, mlp_term.reshape(rank, mats * cols)], axis=1)
    share = halving_scatter(terms, WIDE, wide_count, split_at)
    emb_share = share[:, :long_side]
    mlp_share = share[:, long_side : long_side + mats * cols].reshape(-1, mats, cols)
    emb_first_new, emb_second_new, emb_direction = adam_moments(emb_first, emb_second, emb_share)
    mlp_first_new, mlp_second_new, mlp_direction = adam_moments(mlp_first, mlp_second, mlp_share)
    projected = lax.all_gather(share, WIDE, axis=0, tiled=True)
    directions = jnp.concatenate(
        [emb_direction, mlp_direction.reshape(-1, mats * cols)], axis=1
    )
    directions = lax.all_gather(directions, WIDE, axis=0, tiled=True)
    emb_piece = directions[:, :long_side]
    mlp_piece = directions[:, long_side:].reshape(rank, mats, cols)
    emb_projected = projected[:, :long_side]
    mlp_projected = projected[:, long_side:].reshape(rank, mats, cols)
    emb_total = jnp.dot(emb_basis, emb_piece, precision=matmul_precision)
    mlp_total = jnp.einsum("kdr,rkf->kdf", mlp_basis, mlp_piece, precision=matmul_precision)
    emb_found = jnp.einsum("dv,rv->dr", emb_grad, emb_projected, precision=matmul_precision)
    mlp_found = jnp.einsum("kdf,rkf->dkr", mlp_grad, mlp_projected, precision=matmul_precision)
    found = jnp.concatenate([emb_found, mlp_found.reshape(rows, mats * rank)], axis=1)
    found = exchange_sum(found, "shard", shard_count)
    every = lax.all_gather(found, WIDE, axis=0)
    every = jnp.einsum("tdr,tds->rs", every, every, precision=matmul_precision)
    gram = jnp.stack(
        [every[k * rank : (k + 1) * rank, k * rank : (k + 1) * rank] for k in range(mats + 1)]
    )
    targets = found.reshape(rows, mats + 1, rank).transpose(1, 0, 2)
    basis_new = newton_schulz(targets, gram)
    return (
        emb_total,
        mlp_total,
        emb_first_new,
        emb_second_new,
        mlp_first_new,
        mlp_second_new,
        basis_new[0],
        basis_new[1:],
    )


def solution(mesh):
    placed = (
        P(WIDE, "shard"),
        P(None, WIDE, "shard"),
        P(WIDE, None),
        P(None, WIDE, None),
        P(WIDE, "shard"),
        P(WIDE, "shard"),
        P(WIDE, None, "shard"),
        P(WIDE, None, "shard"),
    )
    return jax.shard_map(
        functools.partial(
            local,
            mesh.shape["shard"],
            mesh.shape["tensor"] * mesh.shape["section"],
            (mesh.shape["section"]).bit_length() - 1,
        ),
        mesh=mesh,
        in_specs=placed,
        out_specs=(
            P(WIDE, "shard"),
            P(None, WIDE, "shard"),
            P(WIDE, "shard"),
            P(WIDE, "shard"),
            P(WIDE, None, "shard"),
            P(WIDE, None, "shard"),
            P(WIDE, None),
            P(None, WIDE, None),
        ),
        check_vma=False,
    )
```

```python
import functools

import jax
import jax.numpy as jnp
from jax import lax
from jax.sharding import PartitionSpec as P

NS_STEPS = 3


coef_a = 3.4445
coef_b = -4.775
coef_c = 2.0315
bias_one = 1.0 - 0.9**10
bias_two = 1.0 - 0.999**10
adam_eps = 1e-08
norm_eps = 1e-07
matmul_precision = lax.Precision.HIGH
WIDE = ("tensor", "section")


def adam_moments(first, second, projected):
    first_new = 0.9 * first + 0.1 * projected
    second_new = 0.999 * second + 0.001 * projected * projected
    direction = first_new / bias_one / (jnp.sqrt(second_new / bias_two) + adam_eps)
    return (first_new, second_new, direction)


def matmul(x, y):
    return jnp.einsum("...rs,...st->...rt", x, y, precision=matmul_precision)


def newton_schulz(target, gram):
    squares = jnp.trace(gram, axis1=-2, axis2=-1)
    scale = 1.0 / (jnp.sqrt(squares) + norm_eps)
    gram_term = gram * (scale * scale)[..., None, None]
    eye = jnp.eye(gram.shape[-1], dtype=gram.dtype)

    def factor_of(gram_term):
        return coef_a * eye + coef_b * gram_term + coef_c * matmul(gram_term, gram_term)

    def sweep(_, carry):
        gram_term, total, factor = carry
        gram_term = matmul(factor, matmul(gram_term, factor))
        factor = factor_of(gram_term)
        return (gram_term, matmul(total, factor), factor)

    factor = factor_of(gram_term)
    _, total, _ = lax.fori_loop(1, NS_STEPS, sweep, (gram_term, factor, factor))
    current = target * scale[..., None, None]
    return matmul(current, total)


def exchange_sum(value, axis, count):
    if count & (count - 1):
        return lax.psum(value, axis)
    step = 1
    while step < count:
        pairs = [(index, index ^ step) for index in range(count)]
        value = value + lax.ppermute(value, axis, pairs)
        step *= 2
    return value


def halving_scatter(value, axis, count, split_at):
    if count & (count - 1):
        return lax.psum_scatter(value, axis, scatter_dimension=0, tiled=True)
    bits = count.bit_length() - 1
    block = value.shape[0] // count
    index = lax.axis_index(axis)
    value = value.reshape((2,) * bits + (block,) + value.shape[1:])
    value, remaining = halving_step(value, list(range(bits - 1, -1, -1)), 0, axis, count, index)
    if bits < 2:
        return value
    cut = value.shape[-1] // 2
    low = list(range(1, split_at))
    high = list(range(split_at, bits))
    first, first_left = value[..., :cut], remaining
    second, second_left = value[..., cut:], remaining
    for bit_a, bit_b in zip(low + high, high + low):
        first, first_left = halving_step(first, first_left, bit_a, axis, count, index)
        second, second_left = halving_step(second, second_left, bit_b, axis, count, index)
    return jnp.concatenate([first, second], axis=-1)


def halving_step(value, remaining, bit, axis, count, index):
    own = (index >> bit) & 1
    axis_at = remaining.index(bit)
    keep = lax.dynamic_index_in_dim(value, own, axis_at, keepdims=False)
    send = lax.dynamic_index_in_dim(value, 1 - own, axis_at, keepdims=False)
    pairs = [(place, place ^ (1 << bit)) for place in range(count)]
    left = [other for other in remaining if other != bit]
    return keep + lax.ppermute(send, axis, pairs), left


def local(shard_count, wide_count, split_at, emb_grad, mlp_grad, emb_basis, mlp_basis, emb_first, emb_second, mlp_first, mlp_second):
    mats, rows, cols = mlp_grad.shape
    long_side = emb_grad.shape[1]
    rank = emb_basis.shape[1]
    emb_term = jnp.einsum("dr,dv->rv", emb_basis, emb_grad, precision=matmul_precision)
    mlp_term = jnp.einsum("kdr,kdf->rkf", mlp_basis, mlp_grad, precision=matmul_precision)
    terms = jnp.concatenate([emb_term, mlp_term.reshape(rank, mats * cols)], axis=1)
    share = halving_scatter(terms, WIDE, wide_count, split_at)
    emb_share = share[:, :long_side]
    mlp_share = share[:, long_side : long_side + mats * cols].reshape(-1, mats, cols)
    emb_first_new, emb_second_new, emb_direction = adam_moments(emb_first, emb_second, emb_share)
    mlp_first_new, mlp_second_new, mlp_direction = adam_moments(mlp_first, mlp_second, mlp_share)
    pieces = jnp.concatenate(
        [
            emb_direction,
            mlp_direction.reshape(-1, mats * cols),
            share,
        ],
        axis=1,
    )
    gathered = lax.all_gather(pieces, WIDE, axis=0, tiled=True)
    width = long_side + mats * cols
    emb_piece = gathered[:, :long_side]
    mlp_piece = gathered[:, long_side:width].reshape(rank, mats, cols)
    emb_projected = gathered[:, width : width + long_side]
    mlp_projected = gathered[:, width + long_side :].reshape(rank, mats, cols)
    emb_total = jnp.dot(emb_basis, emb_piece, precision=matmul_precision)
    mlp_total = jnp.einsum("kdr,rkf->kdf", mlp_basis, mlp_piece, precision=matmul_precision)
    emb_found = jnp.einsum("dv,rv->dr", emb_grad, emb_projected, precision=matmul_precision)
    mlp_found = jnp.einsum("kdf,rkf->dkr", mlp_grad, mlp_projected, precision=matmul_precision)
    found = jnp.concatenate([emb_found, mlp_found.reshape(rows, mats * rank)], axis=1)
    found = exchange_sum(found, "shard", shard_count)
    every = lax.all_gather(found, WIDE, axis=0)
    every = jnp.einsum("tdr,tds->rs", every, every, precision=matmul_precision)
    gram = jnp.stack(
        [every[k * rank : (k + 1) * rank, k * rank : (k + 1) * rank] for k in range(mats + 1)]
    )
    targets = found.reshape(rows, mats + 1, rank).transpose(1, 0, 2)
    basis_new = newton_schulz(targets, gram)
    return (
        emb_total,
        mlp_total,
        emb_first_new,
        emb_second_new,
        mlp_first_new,
        mlp_second_new,
        basis_new[0],
        basis_new[1:],
    )


def solution(mesh):
    placed = (
        P(WIDE, "shard"),
        P(None, WIDE, "shard"),
        P(WIDE, None),
        P(None, WIDE, None),
        P(WIDE, "shard"),
        P(WIDE, "shard"),
        P(WIDE, None, "shard"),
        P(WIDE, None, "shard"),
    )
    return jax.shard_map(
        functools.partial(
            local,
            mesh.shape["shard"],
            mesh.shape["tensor"] * mesh.shape["section"],
            (mesh.shape["section"]).bit_length() - 1,
        ),
        mesh=mesh,
        in_specs=placed,
        out_specs=(
            P(WIDE, "shard"),
            P(None, WIDE, "shard"),
            P(WIDE, "shard"),
            P(WIDE, "shard"),
            P(WIDE, None, "shard"),
            P(WIDE, None, "shard"),
            P(WIDE, None),
            P(None, WIDE, None),
        ),
        check_vma=False,
    )
```

```python
import functools

import jax
import jax.numpy as jnp
from jax import lax
from jax.sharding import PartitionSpec as P

NS_STEPS = 3


coef_a = 3.4445
coef_b = -4.775
coef_c = 2.0315
bias_one = 1.0 - 0.9**10
bias_two = 1.0 - 0.999**10
adam_eps = 1e-08
norm_eps = 1e-07
matmul_precision = lax.Precision.HIGH
WIDE = ("tensor", "section")


def adam_moments(first, second, projected):
    first_new = 0.9 * first + 0.1 * projected
    second_new = 0.999 * second + 0.001 * projected * projected
    direction = first_new / bias_one / (jnp.sqrt(second_new / bias_two) + adam_eps)
    return (first_new, second_new, direction)


def matmul(x, y):
    return jnp.einsum("...rs,...st->...rt", x, y, precision=matmul_precision)


def newton_schulz(target, gram):
    squares = jnp.trace(gram, axis1=-2, axis2=-1)
    scale = 1.0 / (jnp.sqrt(squares) + norm_eps)
    gram_term = gram * (scale * scale)[..., None, None]
    eye = jnp.eye(gram.shape[-1], dtype=gram.dtype)
    total = None
    for sweep_index in range(NS_STEPS):
        factor = coef_a * eye + coef_b * gram_term + coef_c * matmul(gram_term, gram_term)
        if sweep_index + 1 < NS_STEPS:
            gram_term = matmul(factor, matmul(gram_term, factor))
        total = factor if total is None else matmul(total, factor)
    current = target * scale[..., None, None]
    return matmul(current, total)


def exchange_sum(value, axis, count):
    if count & (count - 1):
        return lax.psum(value, axis)
    step = 1
    while step < count:
        pairs = [(index, index ^ step) for index in range(count)]
        value = value + lax.ppermute(value, axis, pairs)
        step *= 2
    return value


def halving_scatter(value, axis, count, split_at):
    if count & (count - 1):
        return lax.psum_scatter(value, axis, scatter_dimension=0, tiled=True)
    bits = count.bit_length() - 1
    block = value.shape[0] // count
    index = lax.axis_index(axis)
    value = value.reshape((2,) * bits + (block,) + value.shape[1:])
    value, remaining = halving_step(value, list(range(bits - 1, -1, -1)), 0, axis, count, index)
    if bits < 2:
        return value
    cut = value.shape[-1] // 2
    low = list(range(1, split_at))
    high = list(range(split_at, bits))
    first, first_left = value[..., :cut], remaining
    second, second_left = value[..., cut:], remaining
    for bit_a, bit_b in zip(low + high, high + low):
        first, first_left = halving_step(first, first_left, bit_a, axis, count, index)
        second, second_left = halving_step(second, second_left, bit_b, axis, count, index)
    return jnp.concatenate([first, second], axis=-1)


def halving_step(value, remaining, bit, axis, count, index):
    own = (index >> bit) & 1
    axis_at = remaining.index(bit)
    keep = lax.dynamic_index_in_dim(value, own, axis_at, keepdims=False)
    send = lax.dynamic_index_in_dim(value, 1 - own, axis_at, keepdims=False)
    pairs = [(place, place ^ (1 << bit)) for place in range(count)]
    left = [other for other in remaining if other != bit]
    return keep + lax.ppermute(send, axis, pairs), left


def local(shard_count, wide_count, split_at, emb_grad, mlp_grad, emb_basis, mlp_basis, emb_first, emb_second, mlp_first, mlp_second):
    mats, rows, cols = mlp_grad.shape
    long_side = emb_grad.shape[1]
    rank = emb_basis.shape[1]
    emb_term = jnp.einsum("dr,dv->rv", emb_basis, emb_grad, precision=matmul_precision)
    mlp_term = jnp.einsum("kdr,kdf->rkf", mlp_basis, mlp_grad, precision=matmul_precision)
    terms = jnp.concatenate([emb_term, mlp_term.reshape(rank, mats * cols)], axis=1)
    share = halving_scatter(terms, WIDE, wide_count, split_at)
    emb_share = share[:, :long_side]
    mlp_share = share[:, long_side : long_side + mats * cols].reshape(-1, mats, cols)
    emb_first_new, emb_second_new, emb_direction = adam_moments(emb_first, emb_second, emb_share)
    mlp_first_new, mlp_second_new, mlp_direction = adam_moments(mlp_first, mlp_second, mlp_share)
    pieces = jnp.concatenate(
        [
            emb_direction,
            mlp_direction.reshape(-1, mats * cols),
            share,
        ],
        axis=1,
    )
    gathered = lax.all_gather(pieces, WIDE, axis=0, tiled=True)
    width = long_side + mats * cols
    emb_piece = gathered[:, :long_side]
    mlp_piece = gathered[:, long_side:width].reshape(rank, mats, cols)
    emb_projected = gathered[:, width : width + long_side]
    mlp_projected = gathered[:, width + long_side :].reshape(rank, mats, cols)
    emb_total = jnp.dot(emb_basis, emb_piece, precision=matmul_precision)
    mlp_total = jnp.einsum("kdr,rkf->kdf", mlp_basis, mlp_piece, precision=matmul_precision)
    emb_found = jnp.einsum("dv,rv->dr", emb_grad, emb_projected, precision=matmul_precision)
    mlp_found = jnp.einsum("kdf,rkf->dkr", mlp_grad, mlp_projected, precision=matmul_precision)
    found = jnp.concatenate([emb_found, mlp_found.reshape(rows, mats * rank)], axis=1)
    found = exchange_sum(found, "shard", shard_count)
    every = lax.all_gather(found, WIDE, axis=0)
    every = jnp.einsum("tdr,tds->rs", every, every, precision=matmul_precision)
    gram = jnp.stack(
        [every[k * rank : (k + 1) * rank, k * rank : (k + 1) * rank] for k in range(mats + 1)]
    )
    targets = found.reshape(rows, mats + 1, rank).transpose(1, 0, 2)
    basis_new = newton_schulz(targets, gram)
    return (
        emb_total,
        mlp_total,
        emb_first_new,
        emb_second_new,
        mlp_first_new,
        mlp_second_new,
        basis_new[0],
        basis_new[1:],
    )


def solution(mesh):
    placed = (
        P(WIDE, "shard"),
        P(None, WIDE, "shard"),
        P(WIDE, None),
        P(None, WIDE, None),
        P(WIDE, "shard"),
        P(WIDE, "shard"),
        P(WIDE, None, "shard"),
        P(WIDE, None, "shard"),
    )
    return jax.shard_map(
        functools.partial(
            local,
            mesh.shape["shard"],
            mesh.shape["tensor"] * mesh.shape["section"],
            (mesh.shape["section"]).bit_length() - 1,
        ),
        mesh=mesh,
        in_specs=placed,
        out_specs=(
            P(WIDE, "shard"),
            P(None, WIDE, "shard"),
            P(WIDE, "shard"),
            P(WIDE, "shard"),
            P(WIDE, None, "shard"),
            P(WIDE, None, "shard"),
            P(WIDE, None),
            P(None, WIDE, None),
        ),
        check_vma=False,
    )
```
